256 devices in a mesh: fsdp: 8 (over z_lo, core), seq: 32 (over x, z_hi, y).
Axes of the slice: x: 4, y: 4, z: 8 (z_hi: 2, z_lo: 4; z = z_hi * 4 + z_lo), core: 2. Of those that a mesh axis runs over, the one named last changes fastest.
Arguments:
- tokens: bfloat16 [2, 4096, 4096], P(None, 'seq'), may hold values from -6 to 6
- positions: int32 [2, 4096], replicated, may hold values from 0 to 4095, as said below
- cached_len: int32 [2], replicated, may hold values from 16 to 4096, as said below
- cache_keys: bfloat16 [2, 4096, 8, 128], P(None, 'seq', 'fsdp'), may hold values from -6 to 6
- cache_values: bfloat16 [2, 4096, 8, 128], P(None, 'seq', 'fsdp'), may hold values from -6 to 6
- w_query: bfloat16 [4096, 4096], P('seq', 'fsdp')
- w_key: bfloat16 [4096, 1024], P('seq', 'fsdp')
- w_value: bfloat16 [4096, 1024], P('seq', 'fsdp'), may hold values from -0.09375 to 0.09375
- w_out_t: bfloat16 [4096, 4096], P('seq', 'fsdp'), may hold values from -1.5 to 1.5
Outputs:
- mixed: bfloat16 [2, 4096, 4096], P(None, 'seq', 'fsdp')
- new_keys: bfloat16 [2, 4096, 8, 128], P(None, 'seq', 'fsdp')
- new_values: bfloat16 [2, 4096, 8, 128], P(None, 'seq', 'fsdp')
The draws below stay inside these ranges and needn't reach their ends.
Inputs may be any that keep to these rules, and one draw needn't show every extreme that they name: For each request the stored order is a permutation of 0 to 4095: the span is cut into 64 blocks of 64 positions, and the 128 stored rows of each index of seq are one block b followed by the block 63 - b, each in rising order; b is drawn per request and index. `cached_len`: some request has exactly 4096 cached positions.
All inputs are finite; a program needn't handle non-finite values.
Results may differ from the reference program's by a relative error of at most 0.015.
The reference program's roundings to bfloat16 on the way (of `queries` and `attended`) count: a program that leaves them out, or rounds other values in their place, can miss the bound.
Values may be sent and summed in bfloat16 or wider, within the bound.
No kernel may reach another device: no remote copies, remote signals or barrier semaphores. Data moves between devices by JAX's collectives and lax.ppermute only.
A program may use at most 128 MiB of HBM per device.

```python
import math
import jax
import jax.numpy as jnp
from jax import lax

D = 4096
HEADS = 32
KV_HEADS = 8
HEAD_DIM = 128
R_TOK = 128
REQ = 2
SINKS = 4
SPAN = 4096
CMAX = 4096
WINDOW = 2048


def query_base(key):
    return jax.random.normal(jax.random.fold_in(key, 11), (D, HEADS * HEAD_DIM), jnp.float32) / math.sqrt(D)


def draw_w_query(key, part):
    return query_base(key).astype(jnp.bfloat16)


def draw_w_key(key, part):
    own_part = jax.random.normal(jax.random.fold_in(key, 12), (D, KV_HEADS * HEAD_DIM), jnp.float32) / math.sqrt(D)
    return own_part.astype(jnp.bfloat16)


def draw_positions(key, part):
    pair_count = SPAN // R_TOK
    half_block = R_TOK // 2
    request_keys = jax.random.split(jax.random.fold_in(key, 21), REQ)
    orders = jax.vmap(lambda one_key: jax.random.permutation(one_key, pair_count))(request_keys)
    orders = orders.astype(jnp.int32)
    offsets = jnp.arange(half_block, dtype=jnp.int32)
    low_rows = orders[:, :, None] * half_block + offsets[None, None, :]
    high_rows = (2 * pair_count - 1 - orders)[:, :, None] * half_block + offsets[None, None, :]
    return jnp.concatenate([low_rows, high_rows], axis=2).reshape(REQ, SPAN).astype(jnp.int32)


def draw_cached_len(key, part):
    drawn = jax.random.randint(jax.random.fold_in(key, 31), (REQ,), 16, CMAX + 1, dtype=jnp.int32)
    longest = jax.random.randint(jax.random.fold_in(key, 32), (), 0, REQ, dtype=jnp.int32)
    return jnp.where(jnp.arange(REQ, dtype=jnp.int32) == longest, CMAX, drawn).astype(jnp.int32)


def levels(rng, dims, cuts, least, top_value):
    loudness = 1.0
    for dim, blocks in cuts:
        draws = jax.random.uniform(jax.random.fold_in(jax.random.fold_in(rng, 6), dim), (blocks,), jnp.float32, least / len(cuts), top_value / len(cuts))
        loudness = loudness * jnp.repeat(jnp.exp(draws), dims[dim] // blocks).reshape((-1,) + (1,) * (len(dims) - 1 - dim))
    return loudness


def noise(key, extent, spread, bound, cuts=(), kind=jnp.bfloat16):
    result = jax.random.normal(key, extent, jnp.float32) * spread
    if len(cuts) > 0:
        result = levels(key, extent, cuts, -0.22, 0.18) * result
    return jnp.clip(result, min=-bound, max=bound).astype(kind)


def setup_inputs(seed: int = 0) -> dict:
    splits = jax.random.split(jax.random.key(seed), 10)
    return {
        "tokens": noise(splits[0], (REQ, SPAN, D), 1.0, 6.0, ((1, 32),)),
        "positions": draw_positions(jax.random.fold_in(splits[9], 71), 0),
        "cached_len": draw_cached_len(jax.random.fold_in(splits[9], 71), 0),
        "cache_keys": noise(splits[3], (REQ, CMAX, KV_HEADS, HEAD_DIM), 1.0, 6.0, ((1, 32), (2, 8))),
        "cache_values": noise(splits[4], (REQ, CMAX, KV_HEADS, HEAD_DIM), 1.0, 6.0, ((1, 32), (2, 8))),
        "w_query": draw_w_query(jax.random.fold_in(splits[9], 71), 0),
        "w_key": draw_w_key(jax.random.fold_in(splits[9], 71), 0),
        "w_value": noise(splits[7], (D, KV_HEADS * HEAD_DIM), D ** -0.5, 0.09375, ((0, 32), (1, 8))),
        "w_out_t": noise(splits[8], (D, HEADS * HEAD_DIM), 16 ** -0.5, 1.5, ((0, 32), (1, 8))),
    }


def reference(tokens, positions, cached_len, cache_keys, cache_values, w_query, w_key, w_value, w_out_t):
    flat_tokens = tokens.reshape(REQ * SPAN, D)
    queries = jnp.dot(flat_tokens, w_query, preferred_element_type=jnp.float32).astype(jnp.bfloat16)
    queries = queries.reshape(REQ, SPAN, HEADS, HEAD_DIM)
    new_keys = jnp.dot(flat_tokens, w_key, preferred_element_type=jnp.float32).astype(jnp.bfloat16)
    new_keys = new_keys.reshape(REQ, SPAN, KV_HEADS, HEAD_DIM)
    new_values = jnp.dot(flat_tokens, w_value, preferred_element_type=jnp.float32).astype(jnp.bfloat16)
    new_values = new_values.reshape(REQ, SPAN, KV_HEADS, HEAD_DIM)
    scale = 1.0 / math.sqrt(HEAD_DIM)
    group_size = HEADS // KV_HEADS
    cache_pos = jnp.arange(CMAX, dtype=jnp.int32)
    results = []
    for request in range(REQ):
        length = cached_len[request]
        query_pos = positions[request]
        cache_mask = (cache_pos[None, :] < length) & ((cache_pos[None, :] < SINKS) | (cache_pos[None, :] > length + query_pos[:, None] - WINDOW))
        before = query_pos[:, None] - query_pos[None, :]
        span_mask = (before >= 0) & (before < WINDOW)
        allowed = jnp.concatenate([cache_mask, span_mask], axis=1)
        all_keys = jnp.concatenate([cache_keys[request], new_keys[request]], axis=0)
        all_values = jnp.concatenate([cache_values[request], new_values[request]], axis=0)
        request_queries = queries[request]

        def one_head(head):
            kv_head = head // group_size
            head_queries = lax.dynamic_index_in_dim(request_queries, head, 1, keepdims=False)
            head_keys = lax.dynamic_index_in_dim(all_keys, kv_head, 1, keepdims=False)
            head_values = lax.dynamic_index_in_dim(all_values, kv_head, 1, keepdims=False)
            scores = jnp.dot(head_queries, head_keys.T, preferred_element_type=jnp.float32) * scale
            scores = jnp.where(allowed, scores, -1e+30)
            largest = lax.optimization_barrier(jnp.max(scores, axis=1, keepdims=True))
            weights = jnp.where(allowed, jnp.exp(scores - largest), 0.0)
            denominator = lax.optimization_barrier(jnp.sum(weights, axis=1, keepdims=True))
            numerator = jnp.dot(weights.astype(jnp.bfloat16), head_values, preferred_element_type=jnp.float32)
            return (numerator / denominator).astype(jnp.bfloat16)
        head_outputs = lax.map(one_head, jnp.arange(HEADS, dtype=jnp.int32))
        results.append(jnp.transpose(head_outputs, (1, 0, 2)).reshape(SPAN, HEADS * HEAD_DIM))
    attended = jnp.stack(results).reshape(REQ * SPAN, HEADS * HEAD_DIM)
    mixed = jnp.dot(attended, w_out_t.T, preferred_element_type=jnp.float32).astype(jnp.bfloat16)
    return (mixed.reshape(REQ, SPAN, D), new_keys, new_values)
```

```python
import math

import jax
import jax.numpy as jnp
from jax import lax
from jax.sharding import Mesh
from jax.sharding import PartitionSpec as P

SINKS = 4
NEGATIVE = -1e30

SEQ = ("x", "z_hi", "y")
FSDP = ("z_lo", "core")


def attend_block(running_state, queries, key_block, value_block, allowed):
    top_old, denom_old, numer_old = running_state
    scores = jnp.einsum("rqkgd,rpkd->rkgqp", queries, key_block, preferred_element_type=jnp.float32)
    scores = scores * (1.0 / math.sqrt(queries.shape[-1]))
    visible = allowed[:, None, None, :, :]
    scores = jnp.where(visible, scores, NEGATIVE)
    top_new = jnp.maximum(top_old, jnp.max(scores, axis=-1))
    rescale = jnp.exp(top_old - top_new)
    weights = jnp.where(visible, jnp.exp(scores - top_new[..., None]), 0.0)
    denom_new = denom_old * rescale + jnp.sum(weights, axis=-1)
    numer_new = numer_old * rescale[..., None] + jnp.einsum(
        "rkgqp,rpkd->rkgqd",
        weights.astype(jnp.bfloat16),
        value_block,
        preferred_element_type=jnp.float32,
    )
    return (top_new, denom_new, numer_new)


def gather_seq(piece, sizes):
    rows, cols = piece.shape
    nx, nz, ny = sizes
    piece = lax.all_gather(piece, "z_hi", axis=0, tiled=False)
    piece = lax.all_gather(piece, ("x", "y"), axis=0, tiled=False)
    piece = piece.reshape(nx, ny, nz, rows, cols).transpose(0, 2, 1, 3, 4)
    return piece.reshape(nx * nz * ny * rows, cols)


def shards(
    sizes, tokens, positions, cached_len, cache_keys, cache_values, w_query, w_key, w_value, w_out_t
):
    requests, rows, width = tokens.shape
    head_size = cache_keys.shape[3]
    kv_local = cache_keys.shape[2]
    group_size = w_query.shape[1] // (kv_local * head_size)
    nx, nz, ny = sizes
    seq_index = (lax.axis_index("x") * nz + lax.axis_index("z_hi")) * ny + lax.axis_index("y")
    seq_count = nx * nz * ny
    window_len = rows * seq_count // 2
    my_positions = lax.dynamic_slice_in_dim(positions, seq_index * rows, rows, 1)
    flat_tokens = tokens.reshape(requests * rows, width)

    q_cols = w_query.shape[1]
    k_cols = w_key.shape[1]
    o_cols = w_out_t.shape[1]
    cache_k_local = jnp.transpose(cache_keys, (1, 0, 2, 3)).reshape(rows, -1)
    cache_v_local = jnp.transpose(cache_values, (1, 0, 2, 3)).reshape(rows, -1)
    packed = jnp.concatenate(
        [w_query, w_key, w_value, w_out_t, cache_k_local, cache_v_local], axis=1
    )
    gathered = gather_seq(packed, sizes)
    total_rows = gathered.shape[0]
    offs = [0]
    for c in (q_cols, k_cols, k_cols, o_cols, cache_k_local.shape[1], cache_v_local.shape[1]):
        offs.append(offs[-1] + c)
    w_qkv = gathered[:, : offs[3]]
    w_out_full = gathered[:, offs[3] : offs[4]]
    cache_k_full = gathered[:, offs[4] : offs[5]].reshape(total_rows, requests, kv_local, head_size)
    cache_v_full = gathered[:, offs[5] : offs[6]].reshape(total_rows, requests, kv_local, head_size)
    cache_k_full = jnp.transpose(cache_k_full, (1, 0, 2, 3))
    cache_v_full = jnp.transpose(cache_v_full, (1, 0, 2, 3))

    qkv_sum = jnp.dot(flat_tokens, w_qkv, preferred_element_type=jnp.float32)
    qkv = qkv_sum.astype(jnp.bfloat16)
    queries = qkv[:, :q_cols].reshape(requests, rows, kv_local, group_size, head_size)
    new_keys = qkv[:, q_cols : q_cols + k_cols].reshape(requests, rows, kv_local, head_size)
    new_values = qkv[:, q_cols + k_cols :].reshape(requests, rows, kv_local, head_size)

    lengths = cached_len[:, None]
    window_floor = lengths + my_positions - window_len
    running_state = (
        jnp.full((requests, kv_local, group_size, rows), NEGATIVE, jnp.float32),
        jnp.zeros((requests, kv_local, group_size, rows), jnp.float32),
        jnp.zeros((requests, kv_local, group_size, rows, head_size), jnp.float32),
    )
    key_pos = jnp.arange(total_rows, dtype=jnp.int32)
    key_pos = key_pos[None, None, :]
    allowed = (key_pos < lengths[:, :, None]) & (
        (key_pos < SINKS) | (key_pos > window_floor[:, :, None])
    )
    running_state = attend_block(running_state, queries, cache_k_full, cache_v_full, allowed)

    new_k_local = jnp.transpose(new_keys, (1, 0, 2, 3)).reshape(rows, -1)
    new_v_local = jnp.transpose(new_values, (1, 0, 2, 3)).reshape(rows, -1)
    new_gathered = gather_seq(jnp.concatenate([new_k_local, new_v_local], axis=1), sizes)
    half = new_k_local.shape[1]
    new_k_full = jnp.transpose(
        new_gathered[:, :half].reshape(total_rows, requests, kv_local, head_size), (1, 0, 2, 3)
    )
    new_v_full = jnp.transpose(
        new_gathered[:, half:].reshape(total_rows, requests, kv_local, head_size), (1, 0, 2, 3)
    )
    before = my_positions[:, :, None] - positions[:, None, :]
    allowed = (before >= 0) & (before < window_len)
    running_state = attend_block(running_state, queries, new_k_full, new_v_full, allowed)
    top_final, denom_final, numer_final = running_state
    attended = (numer_final / denom_final[..., None]).astype(jnp.bfloat16)
    attended = jnp.transpose(attended, (0, 3, 1, 2, 4)).reshape(
        requests * rows, kv_local * group_size * head_size
    )
    partial_out = lax.dot_general(
        attended,
        w_out_full,
        (((1,), (1,)), ((), ())),
        preferred_element_type=jnp.float32,
    )
    mixed = lax.psum_scatter(
        partial_out.reshape(requests, rows, width).astype(jnp.bfloat16),
        FSDP,
        scatter_dimension=2,
        tiled=True,
    )
    return (mixed, new_keys, new_values)


def solution(mesh):
    n_fsdp = mesh.shape["fsdp"]
    n_seq = mesh.shape["seq"]
    n_core = 2
    n_zlo = n_fsdp // n_core
    ny = 4
    nz = 2
    nx = n_seq // (ny * nz)
    fine = Mesh(mesh.devices.reshape(n_zlo, n_core, nx, nz, ny), ("z_lo", "core", "x", "z_hi", "y"))
    placed = (
        P(None, SEQ, None),
        P(),
        P(),
        P(None, SEQ, FSDP, None),
        P(None, SEQ, FSDP, None),
        P(SEQ, FSDP),
        P(SEQ, FSDP),
        P(SEQ, FSDP),
        P(SEQ, FSDP),
    )

    def body(*args):
        return shards((nx, nz, ny), *args)

    return jax.shard_map(
        body,
        mesh=fine,
        in_specs=placed,
        out_specs=(
            P(None, SEQ, FSDP),
            P(None, SEQ, FSDP, None),
            P(None, SEQ, FSDP, None),
        ),
        check_vma=False,
    )
```

```python
import math

import jax
import jax.numpy as jnp
from jax import lax
from jax.sharding import Mesh
from jax.sharding import PartitionSpec as P

SINKS = 4
NEGATIVE = -1e30

SEQ = ("x", "z_hi", "y")
FSDP = ("z_lo", "core")


def z_first_pair(piece, z_index, use_permute):
    if use_permute:
        other = lax.ppermute(piece, "z_hi", [(0, 1), (1, 0)])
        return jnp.where(z_index == 0, jnp.stack([piece, other]), jnp.stack([other, piece]))
    return lax.all_gather(piece, "z_hi", axis=0, tiled=False)


def xy_gather(pair):
    gathered = lax.all_gather(pair, ("x", "y"), axis=0, tiled=False)
    return gathered.reshape(-1, pair.shape[-1])


def to_gather_order(array, axis, sizes):
    nx, nz, ny = sizes
    shape = array.shape
    split = shape[:axis] + (nx, nz, ny, shape[axis] // (nx * nz * ny)) + shape[axis + 1 :]
    perm = list(range(len(split)))
    perm[axis + 1], perm[axis + 2] = perm[axis + 2], perm[axis + 1]
    return jnp.transpose(array.reshape(split), perm).reshape(shape)


def from_gather_order(array, axis, sizes):
    nx, nz, ny = sizes
    shape = array.shape
    split = shape[:axis] + (nx, ny, nz, shape[axis] // (nx * nz * ny)) + shape[axis + 1 :]
    perm = list(range(len(split)))
    perm[axis + 1], perm[axis + 2] = perm[axis + 2], perm[axis + 1]
    return jnp.transpose(array.reshape(split), perm).reshape(shape)


def attend_block(running_state, queries, keys, values, allowed):
    top_old, denom_old, numer_old = running_state
    rows = allowed.shape[0]
    scores = jnp.dot(queries, keys.T, preferred_element_type=jnp.float32)
    scores = scores * (1.0 / math.sqrt(queries.shape[-1]))
    scores = scores.reshape(rows, -1, keys.shape[0])
    visible = allowed[:, None, :]
    scores = jnp.where(visible, scores, NEGATIVE)
    top_new = jnp.maximum(top_old, jnp.max(scores, axis=-1))
    rescale = jnp.exp(top_old - top_new)
    weights = jnp.where(visible, jnp.exp(scores - top_new[..., None]), 0.0)
    denom_new = denom_old * rescale + jnp.sum(weights, axis=-1)
    numer_new = numer_old * rescale[..., None] + jnp.dot(
        weights.astype(jnp.bfloat16).reshape(queries.shape[0], -1),
        values,
        preferred_element_type=jnp.float32,
    ).reshape(numer_old.shape)
    return (top_new, denom_new, numer_new)


def shards(
    sizes, tokens, positions, cached_len, cache_keys, cache_values, w_query, w_key, w_value, w_out_t
):
    requests, rows, width = tokens.shape
    head_size = cache_keys.shape[3]
    kv_local = cache_keys.shape[2]
    group_size = w_query.shape[1] // (kv_local * head_size)
    nx, nz, ny = sizes
    z_index = lax.axis_index("z_hi")
    seq_index = (lax.axis_index("x") * nz + z_index) * ny + lax.axis_index("y")
    seq_count = nx * nz * ny
    total_rows = rows * seq_count
    window_len = total_rows // 2
    my_positions = lax.dynamic_slice_in_dim(positions, seq_index * rows, rows, 1)

    q_cols = w_query.shape[1]
    k_cols = w_key.shape[1]
    o_cols = w_out_t.shape[1]
    kv_cols = kv_local * head_size
    cache_k_local = jnp.transpose(cache_keys, (1, 0, 2, 3)).reshape(rows, -1)
    cache_v_local = jnp.transpose(cache_values, (1, 0, 2, 3)).reshape(rows, -1)
    packed = jnp.concatenate(
        [w_query, w_key, w_value, w_out_t, cache_k_local, cache_v_local], axis=1
    )
    gathered = xy_gather(z_first_pair(packed, z_index, False))
    o_off = q_cols + 2 * k_cols
    ck_off = o_off + o_cols
    cv_off = ck_off + requests * kv_cols

    flat_tokens = to_gather_order(tokens.reshape(requests * rows, width), 1, sizes)
    qkv = jnp.dot(
        flat_tokens, gathered[:, :o_off], preferred_element_type=jnp.float32
    ).astype(jnp.bfloat16)
    queries = qkv[:, :q_cols].reshape(requests, rows, kv_local, group_size, head_size)
    new_keys = qkv[:, q_cols : q_cols + k_cols].reshape(requests, rows, kv_local, head_size)
    new_values = qkv[:, q_cols + k_cols : o_off].reshape(requests, rows, kv_local, head_size)

    new_k_local = jnp.transpose(new_keys, (1, 0, 2, 3)).reshape(rows, -1)
    new_v_local = jnp.transpose(new_values, (1, 0, 2, 3)).reshape(rows, -1)
    new_gathered = xy_gather(
        z_first_pair(jnp.concatenate([new_k_local, new_v_local], axis=1), z_index, True)
    )
    nv_off = requests * kv_cols

    key_pos = to_gather_order(jnp.arange(total_rows, dtype=jnp.int32), 0, sizes)
    new_pos = to_gather_order(positions, 1, sizes)

    outs = []
    for r in range(requests):
        length = cached_len[r]
        t = my_positions[r]
        cache_allowed = (key_pos[None, :] < length) & (
            (key_pos[None, :] < SINKS) | (key_pos[None, :] > (length + t - window_len)[:, None])
        )
        before = t[:, None] - new_pos[r][None, :]
        new_allowed = (before >= 0) & (before < window_len)
        heads = []
        for k in range(kv_local):
            col = (r * kv_local + k) * head_size
            q_rows = queries[r, :, k].reshape(rows * group_size, head_size)
            state = (
                jnp.full((rows, group_size), NEGATIVE, jnp.float32),
                jnp.zeros((rows, group_size), jnp.float32),
                jnp.zeros((rows, group_size, head_size), jnp.float32),
            )
            state = attend_block(
                state,
                q_rows,
                gathered[:, ck_off + col : ck_off + col + head_size],
                gathered[:, cv_off + col : cv_off + col + head_size],
                cache_allowed,
            )
            state = attend_block(
                state,
                q_rows,
                new_gathered[:, col : col + head_size],
                new_gathered[:, nv_off + col : nv_off + col + head_size],
                new_allowed,
            )
            _, denom, numer = state
            heads.append((numer / denom[..., None]).astype(jnp.bfloat16).reshape(rows, -1))
        outs.append(jnp.concatenate(heads, axis=1) if kv_local > 1 else heads[0])
    attended = jnp.concatenate(outs, axis=0)
    partial_out = lax.dot_general(
        attended,
        gathered[:, o_off:ck_off],
        (((1,), (1,)), ((), ())),
        preferred_element_type=jnp.float32,
    )
    partial_out = from_gather_order(partial_out.astype(jnp.bfloat16), 1, sizes)
    mixed = lax.psum_scatter(
        partial_out.reshape(requests, rows, width),
        FSDP,
        scatter_dimension=2,
        tiled=True,
    )
    return (mixed, new_keys, new_values)


def solution(mesh):
    n_fsdp = mesh.shape["fsdp"]
    n_seq = mesh.shape["seq"]
    n_core = 2
    n_zlo = n_fsdp // n_core
    ny = 4
    nz = 2
    nx = n_seq // (ny * nz)
    fine = Mesh(mesh.devices.reshape(n_zlo, n_core, nx, nz, ny), ("z_lo", "core", "x", "z_hi", "y"))
    placed = (
        P(None, SEQ, None),
        P(),
        P(),
        P(None, SEQ, FSDP, None),
        P(None, SEQ, FSDP, None),
        P(SEQ, FSDP),
        P(SEQ, FSDP),
        P(SEQ, FSDP),
        P(SEQ, FSDP),
    )

    def body(*args):
        return shards((nx, nz, ny), *args)

    return jax.shard_map(
        body,
        mesh=fine,
        in_specs=placed,
        out_specs=(
            P(None, SEQ, FSDP),
            P(None, SEQ, FSDP, None),
            P(None, SEQ, FSDP, None),
        ),
        check_vma=False,
    )
```

```python
import math

import jax
import jax.numpy as jnp
from jax import lax
from jax.sharding import Mesh
from jax.sharding import PartitionSpec as P

SINKS = 4
NEGATIVE = -1e30

SEQ = ("x", "z_hi", "y")
FSDP = ("z_lo", "core")


def attend_block(running_state, queries, key_block, value_block, allowed):
    top_old, denom_old, numer_old = running_state
    scores = jnp.einsum("rqkgd,rpkd->rkgqp", queries, key_block, preferred_element_type=jnp.float32)
    scores = scores * (1.0 / math.sqrt(queries.shape[-1]))
    visible = allowed[:, None, None, :, :]
    scores = jnp.where(visible, scores, NEGATIVE)
    top_new = jnp.maximum(top_old, jnp.max(scores, axis=-1))
    rescale = jnp.exp(top_old - top_new)
    weights = jnp.where(visible, jnp.exp(scores - top_new[..., None]), 0.0)
    denom_new = denom_old * rescale + jnp.sum(weights, axis=-1)
    numer_new = numer_old * rescale[..., None] + jnp.einsum(
        "rkgqp,rpkd->rkgqd",
        weights.astype(jnp.bfloat16),
        value_block,
        preferred_element_type=jnp.float32,
    )
    return (top_new, denom_new, numer_new)


def gather_seq(piece, z_index, use_permute):
    if use_permute:
        other = lax.ppermute(piece, "z_hi", [(0, 1), (1, 0)])
        pair = jnp.where(z_index == 0, jnp.stack([piece, other]), jnp.stack([other, piece]))
    else:
        pair = lax.all_gather(piece, "z_hi", axis=0, tiled=False)
    gathered = lax.all_gather(pair, ("x", "y"), axis=0, tiled=False)
    return gathered.reshape(-1, piece.shape[-1])


def to_gather_order(array, axis, sizes):
    nx, nz, ny = sizes
    shape = array.shape
    split = shape[:axis] + (nx, nz, ny, shape[axis] // (nx * nz * ny)) + shape[axis + 1 :]
    perm = list(range(len(split)))
    perm[axis + 1], perm[axis + 2] = perm[axis + 2], perm[axis + 1]
    return jnp.transpose(array.reshape(split), perm).reshape(shape)


def from_gather_order(array, axis, sizes):
    nx, nz, ny = sizes
    shape = array.shape
    split = shape[:axis] + (nx, ny, nz, shape[axis] // (nx * nz * ny)) + shape[axis + 1 :]
    perm = list(range(len(split)))
    perm[axis + 1], perm[axis + 2] = perm[axis + 2], perm[axis + 1]
    return jnp.transpose(array.reshape(split), perm).reshape(shape)


def shards(
    sizes, tokens, positions, cached_len, cache_keys, cache_values, w_query, w_key, w_value, w_out_t
):
    requests, rows, width = tokens.shape
    head_size = cache_keys.shape[3]
    kv_local = cache_keys.shape[2]
    group_size = w_query.shape[1] // (kv_local * head_size)
    nx, nz, ny = sizes
    z_index = lax.axis_index("z_hi")
    seq_index = (lax.axis_index("x") * nz + z_index) * ny + lax.axis_index("y")
    seq_count = nx * nz * ny
    window_len = rows * seq_count // 2
    my_positions = lax.dynamic_slice_in_dim(positions, seq_index * rows, rows, 1)
    flat_tokens = to_gather_order(tokens.reshape(requests * rows, width), 1, sizes)

    q_cols = w_query.shape[1]
    k_cols = w_key.shape[1]
    o_cols = w_out_t.shape[1]
    cache_k_local = jnp.transpose(cache_keys, (1, 0, 2, 3)).reshape(rows, -1)
    cache_v_local = jnp.transpose(cache_values, (1, 0, 2, 3)).reshape(rows, -1)
    packed = jnp.concatenate(
        [w_query, w_key, w_value, w_out_t, cache_k_local, cache_v_local], axis=1
    )
    gathered = gather_seq(packed, z_index, False)
    total_rows = gathered.shape[0]
    offs = [0]
    for c in (q_cols, k_cols, k_cols, o_cols, cache_k_local.shape[1], cache_v_local.shape[1]):
        offs.append(offs[-1] + c)
    w_qkv = gathered[:, : offs[3]]
    w_out_full = gathered[:, offs[3] : offs[4]]
    cache_k_full = gathered[:, offs[4] : offs[5]].reshape(total_rows, requests, kv_local, head_size)
    cache_v_full = gathered[:, offs[5] : offs[6]].reshape(total_rows, requests, kv_local, head_size)
    cache_k_full = jnp.transpose(cache_k_full, (1, 0, 2, 3))
    cache_v_full = jnp.transpose(cache_v_full, (1, 0, 2, 3))

    qkv_sum = jnp.dot(flat_tokens, w_qkv, preferred_element_type=jnp.float32)
    qkv = qkv_sum.astype(jnp.bfloat16)
    queries = qkv[:, :q_cols].reshape(requests, rows, kv_local, group_size, head_size)
    new_keys = qkv[:, q_cols : q_cols + k_cols].reshape(requests, rows, kv_local, head_size)
    new_values = qkv[:, q_cols + k_cols :].reshape(requests, rows, kv_local, head_size)

    lengths = cached_len[:, None]
    window_floor = lengths + my_positions - window_len
    running_state = (
        jnp.full((requests, kv_local, group_size, rows), NEGATIVE, jnp.float32),
        jnp.zeros((requests, kv_local, group_size, rows), jnp.float32),
        jnp.zeros((requests, kv_local, group_size, rows, head_size), jnp.float32),
    )
    key_pos = to_gather_order(jnp.arange(total_rows, dtype=jnp.int32), 0, sizes)
    key_pos = key_pos[None, None, :]
    allowed = (key_pos < lengths[:, :, None]) & (
        (key_pos < SINKS) | (key_pos > window_floor[:, :, None])
    )
    running_state = attend_block(running_state, queries, cache_k_full, cache_v_full, allowed)

    new_k_local = jnp.transpose(new_keys, (1, 0, 2, 3)).reshape(rows, -1)
    new_v_local = jnp.transpose(new_values, (1, 0, 2, 3)).reshape(rows, -1)
    new_gathered = gather_seq(jnp.concatenate([new_k_local, new_v_local], axis=1), z_index, True)
    half = new_k_local.shape[1]
    new_k_full = jnp.transpose(
        new_gathered[:, :half].reshape(total_rows, requests, kv_local, head_size), (1, 0, 2, 3)
    )
    new_v_full = jnp.transpose(
        new_gathered[:, half:].reshape(total_rows, requests, kv_local, head_size), (1, 0, 2, 3)
    )
    new_pos = to_gather_order(positions, 1, sizes)
    before = my_positions[:, :, None] - new_pos[:, None, :]
    allowed = (before >= 0) & (before < window_len)
    running_state = attend_block(running_state, queries, new_k_full, new_v_full, allowed)
    top_final, denom_final, numer_final = running_state
    attended = (numer_final / denom_final[..., None]).astype(jnp.bfloat16)
    attended = jnp.transpose(attended, (0, 3, 1, 2, 4)).reshape(
        requests * rows, kv_local * group_size * head_size
    )
    partial_out = lax.dot_general(
        attended,
        w_out_full,
        (((1,), (1,)), ((), ())),
        preferred_element_type=jnp.float32,
    )
    partial_out = from_gather_order(partial_out.astype(jnp.bfloat16), 1, sizes)
    mixed = lax.psum_scatter(
        partial_out.reshape(requests, rows, width),
        FSDP,
        scatter_dimension=2,
        tiled=True,
    )
    return (mixed, new_keys, new_values)


def solution(mesh):
    n_fsdp = mesh.shape["fsdp"]
    n_seq = mesh.shape["seq"]
    n_core = 2
    n_zlo = n_fsdp // n_core
    ny = 4
    nz = 2
    nx = n_seq // (ny * nz)
    fine = Mesh(mesh.devices.reshape(n_zlo, n_core, nx, nz, ny), ("z_lo", "core", "x", "z_hi", "y"))
    placed = (
        P(None, SEQ, None),
        P(),
        P(),
        P(None, SEQ, FSDP, None),
        P(None, SEQ, FSDP, None),
        P(SEQ, FSDP),
        P(SEQ, FSDP),
        P(SEQ, FSDP),
        P(SEQ, FSDP),
    )

    def body(*args):
        return shards((nx, nz, ny), *args)

    return jax.shard_map(
        body,
        mesh=fine,
        in_specs=placed,
        out_specs=(
            P(None, SEQ, FSDP),
            P(None, SEQ, FSDP, None),
            P(None, SEQ, FSDP, None),
        ),
        check_vma=False,
    )
```

```python
import math

import jax
import jax.numpy as jnp
from jax import lax
from jax.sharding import Mesh
from jax.sharding import PartitionSpec as P

SINKS = 4
NEGATIVE = -1e30

SEQ = ("x", "z_hi", "y")
FSDP = ("z_lo", "core")


def attend_block(running_state, queries, key_block, value_block, allowed):
    top_old, denom_old, numer_old = running_state
    scores = jnp.einsum("rqkgd,rpkd->rkgqp", queries, key_block, preferred_element_type=jnp.float32)
    scores = scores * (1.0 / math.sqrt(queries.shape[-1]))
    visible = allowed[:, None, None, :, :]
    scores = jnp.where(visible, scores, NEGATIVE)
    top_new = jnp.maximum(top_old, jnp.max(scores, axis=-1))
    rescale = jnp.exp(top_old - top_new)
    weights = jnp.where(visible, jnp.exp(scores - top_new[..., None]), 0.0)
    denom_new = denom_old * rescale + jnp.sum(weights, axis=-1)
    numer_new = numer_old * rescale[..., None] + jnp.einsum(
        "rkgqp,rpkd->rkgqd",
        weights.astype(jnp.bfloat16),
        value_block,
        preferred_element_type=jnp.float32,
    )
    return (top_new, denom_new, numer_new)


def gather_seq(piece, z_index, use_permute):
    if use_permute:
        other = lax.ppermute(piece, "z_hi", [(0, 1), (1, 0)])
        pair = jnp.where(z_index == 0, jnp.stack([piece, other]), jnp.stack([other, piece]))
    else:
        pair = lax.all_gather(piece, "z_hi", axis=0, tiled=False)
    gathered = lax.all_gather(pair, ("x", "y"), axis=0, tiled=False)
    return gathered.reshape(-1, piece.shape[-1])


def to_gather_order(array, axis, sizes):
    nx, nz, ny = sizes
    shape = array.shape
    split = shape[:axis] + (nx, nz, ny, shape[axis] // (nx * nz * ny)) + shape[axis + 1 :]
    perm = list(range(len(split)))
    perm[axis + 1], perm[axis + 2] = perm[axis + 2], perm[axis + 1]
    return jnp.transpose(array.reshape(split), perm).reshape(shape)


def from_gather_order(array, axis, sizes):
    nx, nz, ny = sizes
    shape = array.shape
    split = shape[:axis] + (nx, ny, nz, shape[axis] // (nx * nz * ny)) + shape[axis + 1 :]
    perm = list(range(len(split)))
    perm[axis + 1], perm[axis + 2] = perm[axis + 2], perm[axis + 1]
    return jnp.transpose(array.reshape(split), perm).reshape(shape)


def shards(
    sizes, tokens, positions, cached_len, cache_keys, cache_values, w_query, w_key, w_value, w_out_t
):
    requests, rows, width = tokens.shape
    head_size = cache_keys.shape[3]
    kv_local = cache_keys.shape[2]
    group_size = w_query.shape[1] // (kv_local * head_size)
    nx, nz, ny = sizes
    z_index = lax.axis_index("z_hi")
    seq_index = (lax.axis_index("x") * nz + z_index) * ny + lax.axis_index("y")
    seq_count = nx * nz * ny
    window_len = rows * seq_count // 2
    my_positions = lax.dynamic_slice_in_dim(positions, seq_index * rows, rows, 1)
    flat_tokens = to_gather_order(tokens.reshape(requests * rows, width), 1, sizes)

    q_cols = w_query.shape[1]
    k_cols = w_key.shape[1]
    o_cols = w_out_t.shape[1]
    cache_k_local = jnp.transpose(cache_keys, (1, 0, 2, 3)).reshape(rows, -1)
    cache_v_local = jnp.transpose(cache_values, (1, 0, 2, 3)).reshape(rows, -1)
    packed = jnp.concatenate(
        [w_query, w_key, w_value, w_out_t, cache_k_local, cache_v_local], axis=1
    )
    gathered = gather_seq(packed, z_index, False)
    total_rows = gathered.shape[0]
    offs = [0]
    for c in (q_cols, k_cols, k_cols, o_cols, cache_k_local.shape[1], cache_v_local.shape[1]):
        offs.append(offs[-1] + c)
    w_qkv = gathered[:, : offs[3]]
    w_out_full = from_gather_order(gathered[:, offs[3] : offs[4]], 0, sizes)
    kv_cols = kv_local * head_size

    qkv_sum = jnp.dot(flat_tokens, w_qkv, preferred_element_type=jnp.float32)
    qkv = qkv_sum.astype(jnp.bfloat16)
    queries = qkv[:, :q_cols].reshape(requests, rows, kv_local, group_size, head_size)
    new_keys = qkv[:, q_cols : q_cols + k_cols].reshape(requests, rows, kv_local, head_size)
    new_values = qkv[:, q_cols + k_cols :].reshape(requests, rows, kv_local, head_size)

    new_k_local = jnp.transpose(new_keys, (1, 0, 2, 3)).reshape(rows, -1)
    new_v_local = jnp.transpose(new_values, (1, 0, 2, 3)).reshape(rows, -1)
    new_gathered = gather_seq(jnp.concatenate([new_k_local, new_v_local], axis=1), z_index, True)
    half = new_k_local.shape[1]

    key_pos = to_gather_order(jnp.arange(total_rows, dtype=jnp.int32), 0, sizes)
    key_pos = key_pos[None, None, :]
    new_pos = to_gather_order(positions, 1, sizes)
    lengths = cached_len[:, None]
    window_floor = lengths + my_positions - window_len
    cache_allowed = (key_pos < lengths[:, :, None]) & (
        (key_pos < SINKS) | (key_pos > window_floor[:, :, None])
    )
    before = my_positions[:, :, None] - new_pos[:, None, :]
    new_allowed = (before >= 0) & (before < window_len)

    def block_of(source, offset, r):
        piece = source[:, offset + r * kv_cols : offset + (r + 1) * kv_cols]
        return piece.reshape(1, total_rows, kv_local, head_size)

    attended_parts = []
    for r in range(requests):
        running_state = (
            jnp.full((1, kv_local, group_size, rows), NEGATIVE, jnp.float32),
            jnp.zeros((1, kv_local, group_size, rows), jnp.float32),
            jnp.zeros((1, kv_local, group_size, rows, head_size), jnp.float32),
        )
        q_r = queries[r : r + 1]
        running_state = attend_block(
            running_state,
            q_r,
            block_of(gathered, offs[4], r),
            block_of(gathered, offs[5], r),
            cache_allowed[r : r + 1],
        )
        running_state = attend_block(
            running_state,
            q_r,
            block_of(new_gathered, 0, r),
            block_of(new_gathered, half, r),
            new_allowed[r : r + 1],
        )
        _, denom_final, numer_final = running_state
        attended_r = (numer_final / denom_final[..., None]).astype(jnp.bfloat16)
        attended_parts.append(
            jnp.transpose(attended_r, (0, 3, 1, 2, 4)).reshape(
                rows, kv_local * group_size * head_size
            )
        )
    attended = jnp.concatenate(attended_parts, axis=0)
    partial_out = lax.dot_general(
        attended,
        w_out_full,
        (((1,), (1,)), ((), ())),
        preferred_element_type=jnp.float32,
    )
    mixed = lax.psum_scatter(
        partial_out.reshape(requests, rows, width).astype(jnp.bfloat16),
        FSDP,
        scatter_dimension=2,
        tiled=True,
    )
    return (mixed, new_keys, new_values)


def solution(mesh):
    n_fsdp = mesh.shape["fsdp"]
    n_seq = mesh.shape["seq"]
    n_core = 2
    n_zlo = n_fsdp // n_core
    ny = 4
    nz = 2
    nx = n_seq // (ny * nz)
    fine = Mesh(mesh.devices.reshape(n_zlo, n_core, nx, nz, ny), ("z_lo", "core", "x", "z_hi", "y"))
    placed = (
        P(None, SEQ, None),
        P(),
        P(),
        P(None, SEQ, FSDP, None),
        P(None, SEQ, FSDP, None),
        P(SEQ, FSDP),
        P(SEQ, FSDP),
        P(SEQ, FSDP),
        P(SEQ, FSDP),
    )

    def body(*args):
        return shards((nx, nz, ny), *args)

    return jax.shard_map(
        body,
        mesh=fine,
        in_specs=placed,
        out_specs=(
            P(None, SEQ, FSDP),
            P(None, SEQ, FSDP, None),
            P(None, SEQ, FSDP, None),
        ),
        check_vma=False,
    )
```

```python
import math

import jax
import jax.numpy as jnp
from jax import lax
from jax.sharding import Mesh
from jax.sharding import PartitionSpec as P

SINKS = 4
NEGATIVE = -1e30

SEQ = ("x", "z_hi", "y")
FSDP = ("z_lo", "core")


def attend_block(running_state, queries, key_block, value_block, allowed):
    top_old, denom_old, numer_old = running_state
    scores = jnp.einsum("rqkgd,rpkd->rkgqp", queries, key_block, preferred_element_type=jnp.float32)
    scores = scores * (1.0 / math.sqrt(queries.shape[-1]))
    visible = allowed[:, None, None, :, :]
    scores = jnp.where(visible, scores, NEGATIVE)
    top_new = jnp.maximum(top_old, jnp.max(scores, axis=-1))
    rescale = jnp.exp(top_old - top_new)
    weights = jnp.exp(scores - top_new[..., None])
    denom_new = denom_old * rescale + jnp.sum(weights, axis=-1)
    numer_new = numer_old * rescale[..., None] + jnp.einsum(
        "rkgqp,rpkd->rkgqd",
        weights.astype(jnp.bfloat16),
        value_block,
        preferred_element_type=jnp.float32,
    )
    return (top_new, denom_new, numer_new)


def gather_seq(piece, z_index, use_permute):
    if use_permute:
        other = lax.ppermute(piece, "z_hi", [(0, 1), (1, 0)])
        pair = jnp.where(z_index == 0, jnp.stack([piece, other]), jnp.stack([other, piece]))
    else:
        pair = lax.all_gather(piece, "z_hi", axis=0, tiled=False)
    gathered = lax.all_gather(pair, ("x", "y"), axis=0, tiled=False)
    return gathered.reshape(-1, piece.shape[-1])


def to_gather_order(array, axis, sizes):
    nx, nz, ny = sizes
    shape = array.shape
    split = shape[:axis] + (nx, nz, ny, shape[axis] // (nx * nz * ny)) + shape[axis + 1 :]
    perm = list(range(len(split)))
    perm[axis + 1], perm[axis + 2] = perm[axis + 2], perm[axis + 1]
    return jnp.transpose(array.reshape(split), perm).reshape(shape)


def from_gather_order(array, axis, sizes):
    nx, nz, ny = sizes
    shape = array.shape
    split = shape[:axis] + (nx, ny, nz, shape[axis] // (nx * nz * ny)) + shape[axis + 1 :]
    perm = list(range(len(split)))
    perm[axis + 1], perm[axis + 2] = perm[axis + 2], perm[axis + 1]
    return jnp.transpose(array.reshape(split), perm).reshape(shape)


def shards(
    sizes, tokens, positions, cached_len, cache_keys, cache_values, w_query, w_key, w_value, w_out_t
):
    requests, rows, width = tokens.shape
    head_size = cache_keys.shape[3]
    kv_local = cache_keys.shape[2]
    group_size = w_query.shape[1] // (kv_local * head_size)
    nx, nz, ny = sizes
    z_index = lax.axis_index("z_hi")
    seq_index = (lax.axis_index("x") * nz + z_index) * ny + lax.axis_index("y")
    seq_count = nx * nz * ny
    window_len = rows * seq_count // 2
    my_positions = lax.dynamic_slice_in_dim(positions, seq_index * rows, rows, 1)
    flat_tokens = to_gather_order(tokens.reshape(requests * rows, width), 1, sizes)

    q_cols = w_query.shape[1]
    k_cols = w_key.shape[1]
    o_cols = w_out_t.shape[1]
    cache_k_local = jnp.transpose(cache_keys, (1, 0, 2, 3)).reshape(rows, -1)
    cache_v_local = jnp.transpose(cache_values, (1, 0, 2, 3)).reshape(rows, -1)
    packed = jnp.concatenate(
        [w_query, w_key, w_value, w_out_t, cache_k_local, cache_v_local], axis=1
    )
    gathered = gather_seq(packed, z_index, False)
    total_rows = gathered.shape[0]
    offs = [0]
    for c in (q_cols, k_cols, k_cols, o_cols, cache_k_local.shape[1], cache_v_local.shape[1]):
        offs.append(offs[-1] + c)
    w_qkv = gathered[:, : offs[3]]
    w_out_full = from_gather_order(gathered[:, offs[3] : offs[4]], 0, sizes)
    kv_cols = kv_local * head_size

    qkv_sum = jnp.dot(flat_tokens, w_qkv, preferred_element_type=jnp.float32)
    qkv = qkv_sum.astype(jnp.bfloat16)
    queries = qkv[:, :q_cols].reshape(requests, rows, kv_local, group_size, head_size)
    new_keys = qkv[:, q_cols : q_cols + k_cols].reshape(requests, rows, kv_local, head_size)
    new_values = qkv[:, q_cols + k_cols :].reshape(requests, rows, kv_local, head_size)

    new_k_local = jnp.transpose(new_keys, (1, 0, 2, 3)).reshape(rows, -1)
    new_v_local = jnp.transpose(new_values, (1, 0, 2, 3)).reshape(rows, -1)
    new_gathered = gather_seq(jnp.concatenate([new_k_local, new_v_local], axis=1), z_index, True)
    half = new_k_local.shape[1]

    key_pos = to_gather_order(jnp.arange(total_rows, dtype=jnp.int32), 0, sizes)
    key_pos = key_pos[None, None, :]
    new_pos = to_gather_order(positions, 1, sizes)
    lengths = cached_len[:, None]
    window_floor = lengths + my_positions - window_len
    cache_allowed = (key_pos < lengths[:, :, None]) & (
        (key_pos < SINKS) | (key_pos > window_floor[:, :, None])
    )
    before = my_positions[:, :, None] - new_pos[:, None, :]
    new_allowed = (before >= 0) & (before < window_len)

    def block_of(source, offset, r):
        piece = source[:, offset + r * kv_cols : offset + (r + 1) * kv_cols]
        return piece.reshape(1, total_rows, kv_local, head_size)

    attended_parts = []
    for r in range(requests):
        running_state = (
            jnp.full((1, kv_local, group_size, rows), NEGATIVE, jnp.float32),
            jnp.zeros((1, kv_local, group_size, rows), jnp.float32),
            jnp.zeros((1, kv_local, group_size, rows, head_size), jnp.float32),
        )
        q_r = queries[r : r + 1]
        running_state = attend_block(
            running_state,
            q_r,
            block_of(gathered, offs[4], r),
            block_of(gathered, offs[5], r),
            cache_allowed[r : r + 1],
        )
        running_state = attend_block(
            running_state,
            q_r,
            block_of(new_gathered, 0, r),
            block_of(new_gathered, half, r),
            new_allowed[r : r + 1],
        )
        _, denom_final, numer_final = running_state
        attended_r = (numer_final / denom_final[..., None]).astype(jnp.bfloat16)
        attended_parts.append(
            jnp.transpose(attended_r, (0, 3, 1, 2, 4)).reshape(
                rows, kv_local * group_size * head_size
            )
        )
    attended = jnp.concatenate(attended_parts, axis=0)
    partial_out = lax.dot_general(
        attended,
        w_out_full,
        (((1,), (1,)), ((), ())),
        preferred_element_type=jnp.float32,
    )
    mixed = lax.psum_scatter(
        partial_out.reshape(requests, rows, width).astype(jnp.bfloat16),
        FSDP,
        scatter_dimension=2,
        tiled=True,
    )
    return (mixed, new_keys, new_values)


def solution(mesh):
    n_fsdp = mesh.shape["fsdp"]
    n_seq = mesh.shape["seq"]
    n_core = 2
    n_zlo = n_fsdp // n_core
    ny = 4
    nz = 2
    nx = n_seq // (ny * nz)
    fine = Mesh(mesh.devices.reshape(n_zlo, n_core, nx, nz, ny), ("z_lo", "core", "x", "z_hi", "y"))
    placed = (
        P(None, SEQ, None),
        P(),
        P(),
        P(None, SEQ, FSDP, None),
        P(None, SEQ, FSDP, None),
        P(SEQ, FSDP),
        P(SEQ, FSDP),
        P(SEQ, FSDP),
        P(SEQ, FSDP),
    )

    def body(*args):
        return shards((nx, nz, ny), *args)

    return jax.shard_map(
        body,
        mesh=fine,
        in_specs=placed,
        out_specs=(
            P(None, SEQ, FSDP),
            P(None, SEQ, FSDP, None),
            P(None, SEQ, FSDP, None),
        ),
        check_vma=False,
    )
```

```python
import math

import jax
import jax.numpy as jnp
from jax import lax
from jax.sharding import Mesh
from jax.sharding import PartitionSpec as P


SINKS = 4
NEGATIVE = -1e30

SEQ = ("x", "z_hi", "y")
FSDP = ("z_lo", "core")


def attend_block(running_state, queries, key_block, value_block, allowed):
    top_old, denom_old, numer_old = running_state
    scores = jnp.einsum("rqkgd,rpkd->rkgqp", queries, key_block, preferred_element_type=jnp.float32)
    scores = scores * (1.0 / math.sqrt(queries.shape[-1]))
    visible = allowed[:, None, None, :, :]
    scores = jnp.where(visible, scores, NEGATIVE)
    top_new = jnp.maximum(top_old, jnp.max(scores, axis=-1))
    rescale = jnp.exp(top_old - top_new)
    weights = jnp.exp(scores - top_new[..., None])
    denom_new = denom_old * rescale + jnp.sum(weights, axis=-1)
    numer_new = numer_old * rescale[..., None] + jnp.einsum(
        "rkgqp,rpkd->rkgqd",
        weights.astype(jnp.bfloat16),
        value_block,
        preferred_element_type=jnp.float32,
    )
    return (top_new, denom_new, numer_new)


def gather_seq(piece, z_index, use_permute):
    if use_permute:
        other = lax.ppermute(piece, "z_hi", [(0, 1), (1, 0)])
        pair = jnp.where(z_index == 0, jnp.stack([piece, other]), jnp.stack([other, piece]))
    else:
        pair = lax.all_gather(piece, "z_hi", axis=0, tiled=False)
    gathered = lax.all_gather(pair, ("x", "y"), axis=0, tiled=False)
    return gathered.reshape(-1, piece.shape[-1])


def to_gather_order(array, axis, sizes):
    nx, nz, ny = sizes
    shape = array.shape
    split = shape[:axis] + (nx, nz, ny, shape[axis] // (nx * nz * ny)) + shape[axis + 1 :]
    perm = list(range(len(split)))
    perm[axis + 1], perm[axis + 2] = perm[axis + 2], perm[axis + 1]
    return jnp.transpose(array.reshape(split), perm).reshape(shape)


def from_gather_order(array, axis, sizes):
    nx, nz, ny = sizes
    shape = array.shape
    split = shape[:axis] + (nx, ny, nz, shape[axis] // (nx * nz * ny)) + shape[axis + 1 :]
    perm = list(range(len(split)))
    perm[axis + 1], perm[axis + 2] = perm[axis + 2], perm[axis + 1]
    return jnp.transpose(array.reshape(split), perm).reshape(shape)


def shards(
    sizes, tokens, positions, cached_len, cache_keys, cache_values, w_query, w_key, w_value, w_out_t
):
    requests, rows, width = tokens.shape
    head_size = cache_keys.shape[3]
    kv_local = cache_keys.shape[2]
    group_size = w_query.shape[1] // (kv_local * head_size)
    nx, nz, ny = sizes
    z_index = lax.axis_index("z_hi")
    seq_index = (lax.axis_index("x") * nz + z_index) * ny + lax.axis_index("y")
    seq_count = nx * nz * ny
    window_len = rows * seq_count // 2
    my_positions = lax.dynamic_slice_in_dim(positions, seq_index * rows, rows, 1)
    flat_tokens = to_gather_order(tokens.reshape(requests * rows, width), 1, sizes)

    q_cols = w_query.shape[1]
    k_cols = w_key.shape[1]
    o_cols = w_out_t.shape[1]
    cache_k_local = jnp.transpose(cache_keys, (1, 0, 2, 3)).reshape(rows, -1)
    cache_v_local = jnp.transpose(cache_values, (1, 0, 2, 3)).reshape(rows, -1)
    packed = jnp.concatenate(
        [w_query, w_key, w_value, w_out_t, cache_k_local, cache_v_local], axis=1
    )
    gathered = gather_seq(packed, z_index, False)
    total_rows = gathered.shape[0]
    offs = [0]
    for c in (q_cols, k_cols, k_cols, o_cols, cache_k_local.shape[1], cache_v_local.shape[1]):
        offs.append(offs[-1] + c)
    w_qkv = gathered[:, : offs[3]]
    w_out_full = from_gather_order(gathered[:, offs[3] : offs[4]], 0, sizes)
    kv_cols = kv_local * head_size

    kv_new = jnp.dot(
        flat_tokens, w_qkv[:, q_cols:], preferred_element_type=jnp.float32
    ).astype(jnp.bfloat16)
    new_keys = kv_new[:, :k_cols].reshape(requests, rows, kv_local, head_size)
    new_values = kv_new[:, k_cols:].reshape(requests, rows, kv_local, head_size)
    queries = jnp.dot(
        flat_tokens, w_qkv[:, :q_cols], preferred_element_type=jnp.float32
    ).astype(jnp.bfloat16)
    queries = queries.reshape(requests, rows, kv_local, group_size, head_size)

    new_k_local = jnp.transpose(new_keys, (1, 0, 2, 3)).reshape(rows, -1)
    new_v_local = jnp.transpose(new_values, (1, 0, 2, 3)).reshape(rows, -1)
    new_gathered = gather_seq(jnp.concatenate([new_k_local, new_v_local], axis=1), z_index, True)
    half = new_k_local.shape[1]

    key_pos = to_gather_order(jnp.arange(total_rows, dtype=jnp.int32), 0, sizes)
    key_pos = key_pos[None, None, :]
    new_pos = to_gather_order(positions, 1, sizes)
    lengths = cached_len[:, None]
    window_floor = lengths + my_positions - window_len
    cache_allowed = (key_pos < lengths[:, :, None]) & (
        (key_pos < SINKS) | (key_pos > window_floor[:, :, None])
    )
    before = my_positions[:, :, None] - new_pos[:, None, :]
    new_allowed = (before >= 0) & (before < window_len)

    def block_of(source, offset, r):
        piece = source[:, offset + r * kv_cols : offset + (r + 1) * kv_cols]
        return piece.reshape(1, total_rows, kv_local, head_size)

    attended_parts = []
    for r in range(requests):
        running_state = (
            jnp.full((1, kv_local, group_size, rows), NEGATIVE, jnp.float32),
            jnp.zeros((1, kv_local, group_size, rows), jnp.float32),
            jnp.zeros((1, kv_local, group_size, rows, head_size), jnp.float32),
        )
        q_r = queries[r : r + 1]
        running_state = attend_block(
            running_state,
            q_r,
            block_of(gathered, offs[4], r),
            block_of(gathered, offs[5], r),
            cache_allowed[r : r + 1],
        )
        running_state = attend_block(
            running_state,
            q_r,
            block_of(new_gathered, 0, r),
            block_of(new_gathered, half, r),
            new_allowed[r : r + 1],
        )
        _, denom_final, numer_final = running_state
        attended_r = (numer_final / denom_final[..., None]).astype(jnp.bfloat16)
        attended_parts.append(
            jnp.transpose(attended_r, (0, 3, 1, 2, 4)).reshape(
                rows, kv_local * group_size * head_size
            )
        )
    attended = jnp.concatenate(attended_parts, axis=0)
    partial_out = lax.dot_general(
        attended,
        w_out_full,
        (((1,), (1,)), ((), ())),
        preferred_element_type=jnp.float32,
    )
    mixed = lax.psum_scatter(
        partial_out.reshape(requests, rows, width).astype(jnp.bfloat16),
        FSDP,
        scatter_dimension=2,
        tiled=True,
    )
    return (mixed, new_keys, new_values)


def solution(mesh):
    n_fsdp = mesh.shape["fsdp"]
    n_seq = mesh.shape["seq"]
    n_core = 2
    n_zlo = n_fsdp // n_core
    ny = 4
    nz = 2
    nx = n_seq // (ny * nz)
    fine = Mesh(mesh.devices.reshape(n_zlo, n_core, nx, nz, ny), ("z_lo", "core", "x", "z_hi", "y"))
    placed = (
        P(None, SEQ, None),
        P(),
        P(),
        P(None, SEQ, FSDP, None),
        P(None, SEQ, FSDP, None),
        P(SEQ, FSDP),
        P(SEQ, FSDP),
        P(SEQ, FSDP),
        P(SEQ, FSDP),
    )

    def body(*args):
        return shards((nx, nz, ny), *args)

    return jax.shard_map(
        body,
        mesh=fine,
        in_specs=placed,
        out_specs=(
            P(None, SEQ, FSDP),
            P(None, SEQ, FSDP, None),
            P(None, SEQ, FSDP, None),
        ),
        check_vma=False,
    )
```

```python
import math

import jax
import jax.numpy as jnp
from jax import lax
from jax.sharding import Mesh
from jax.sharding import PartitionSpec as P


SINKS = 4
NEGATIVE = -1e30

SEQ = ("x", "z_hi", "y")
FSDP = ("z_lo", "core")


def attend_block(running_state, queries, key_block, value_block, allowed):
    top_old, denom_old, numer_old = running_state
    scores = jnp.einsum("rqkgd,rpkd->rkgqp", queries, key_block, preferred_element_type=jnp.float32)
    scores = scores * (1.0 / math.sqrt(queries.shape[-1]))
    visible = allowed[:, None, None, :, :]
    scores = jnp.where(visible, scores, NEGATIVE)
    top_new = jnp.maximum(top_old, jnp.max(scores, axis=-1))
    rescale = jnp.exp(top_old - top_new)
    weights = jnp.exp(scores - top_new[..., None])
    denom_new = denom_old * rescale + jnp.sum(weights, axis=-1)
    numer_new = numer_old * rescale[..., None] + jnp.einsum(
        "rkgqp,rpkd->rkgqd",
        weights.astype(jnp.bfloat16),
        value_block,
        preferred_element_type=jnp.float32,
    )
    return (top_new, denom_new, numer_new)


def gather_seq(piece, z_index, use_permute):
    if use_permute:
        other = lax.ppermute(piece, "z_hi", [(0, 1), (1, 0)])
        pair = jnp.where(z_index == 0, jnp.stack([piece, other]), jnp.stack([other, piece]))
    else:
        pair = lax.all_gather(piece, "z_hi", axis=0, tiled=False)
    gathered = lax.all_gather(pair, ("x", "y"), axis=0, tiled=False)
    return gathered.reshape(-1, piece.shape[-1])


def to_gather_order(array, axis, sizes):
    nx, nz, ny = sizes
    shape = array.shape
    split = shape[:axis] + (nx, nz, ny, shape[axis] // (nx * nz * ny)) + shape[axis + 1 :]
    perm = list(range(len(split)))
    perm[axis + 1], perm[axis + 2] = perm[axis + 2], perm[axis + 1]
    return jnp.transpose(array.reshape(split), perm).reshape(shape)


def from_gather_order(array, axis, sizes):
    nx, nz, ny = sizes
    shape = array.shape
    split = shape[:axis] + (nx, ny, nz, shape[axis] // (nx * nz * ny)) + shape[axis + 1 :]
    perm = list(range(len(split)))
    perm[axis + 1], perm[axis + 2] = perm[axis + 2], perm[axis + 1]
    return jnp.transpose(array.reshape(split), perm).reshape(shape)


def shards(
    sizes, tokens, positions, cached_len, cache_keys, cache_values, w_query, w_key, w_value, w_out_t
):
    requests, rows, width = tokens.shape
    head_size = cache_keys.shape[3]
    kv_local = cache_keys.shape[2]
    group_size = w_query.shape[1] // (kv_local * head_size)
    nx, nz, ny = sizes
    z_index = lax.axis_index("z_hi")
    seq_index = (lax.axis_index("x") * nz + z_index) * ny + lax.axis_index("y")
    seq_count = nx * nz * ny
    window_len = rows * seq_count // 2
    my_positions = lax.dynamic_slice_in_dim(positions, seq_index * rows, rows, 1)
    flat_tokens = to_gather_order(tokens.reshape(requests * rows, width), 1, sizes)

    q_cols = w_query.shape[1]
    k_cols = w_key.shape[1]
    o_cols = w_out_t.shape[1]
    cache_k_local = jnp.transpose(cache_keys, (1, 0, 2, 3)).reshape(rows, -1)
    cache_v_local = jnp.transpose(cache_values, (1, 0, 2, 3)).reshape(rows, -1)
    packed = jnp.concatenate(
        [w_query, w_key, w_value, w_out_t, cache_k_local, cache_v_local], axis=1
    )
    gathered = gather_seq(packed, z_index, False)
    total_rows = gathered.shape[0]
    offs = [0]
    for c in (q_cols, k_cols, k_cols, o_cols, cache_k_local.shape[1], cache_v_local.shape[1]):
        offs.append(offs[-1] + c)
    w_qkv = gathered[:, : offs[3]]
    w_out_full = from_gather_order(gathered[:, offs[3] : offs[4]], 0, sizes)
    kv_cols = kv_local * head_size

    kv_new = jnp.dot(
        flat_tokens, w_qkv[:, q_cols:], preferred_element_type=jnp.float32
    ).astype(jnp.bfloat16)
    new_keys = kv_new[:, :k_cols].reshape(requests, rows, kv_local, head_size)
    new_values = kv_new[:, k_cols:].reshape(requests, rows, kv_local, head_size)
    queries = jnp.dot(
        flat_tokens, w_qkv[:, :q_cols], preferred_element_type=jnp.float32
    ).astype(jnp.bfloat16)
    queries = queries.reshape(requests, rows, kv_local, group_size, head_size)

    new_k_local = jnp.transpose(new_keys, (1, 0, 2, 3)).reshape(rows, -1)
    new_v_local = jnp.transpose(new_values, (1, 0, 2, 3)).reshape(rows, -1)
    new_gathered = gather_seq(jnp.concatenate([new_k_local, new_v_local], axis=1), z_index, True)
    half = new_k_local.shape[1]

    key_pos = to_gather_order(jnp.arange(total_rows, dtype=jnp.int32), 0, sizes)
    key_pos = key_pos[None, None, :]
    new_pos = to_gather_order(positions, 1, sizes)
    lengths = cached_len[:, None]
    window_floor = lengths + my_positions - window_len
    cache_allowed = (key_pos < lengths[:, :, None]) & (
        (key_pos < SINKS) | (key_pos > window_floor[:, :, None])
    )
    blk = rows // 2
    n_blocks = total_rows // blk
    window_blocks = window_len // blk + 1

    def block_of(source, offset, r):
        piece = source[:, offset + r * kv_cols : offset + (r + 1) * kv_cols]
        return piece.reshape(1, total_rows, kv_local, head_size)

    attended_parts = []
    for r in range(requests):
        running_state = (
            jnp.full((1, kv_local, group_size, rows), NEGATIVE, jnp.float32),
            jnp.zeros((1, kv_local, group_size, rows), jnp.float32),
            jnp.zeros((1, kv_local, group_size, rows, head_size), jnp.float32),
        )
        q_r = queries[r : r + 1]
        running_state = attend_block(
            running_state,
            q_r,
            block_of(gathered, offs[4], r),
            block_of(gathered, offs[5], r),
            cache_allowed[r : r + 1],
        )
        keys_r = block_of(new_gathered, 0, r).reshape(n_blocks, blk, kv_local, head_size)
        values_r = block_of(new_gathered, half, r).reshape(n_blocks, blk, kv_local, head_size)
        pos_blocks = new_pos[r].reshape(n_blocks, blk)
        slot_of_block = (
            jnp.zeros((n_blocks,), jnp.int32)
            .at[pos_blocks[:, 0] // blk]
            .set(jnp.arange(n_blocks, dtype=jnp.int32))
        )
        halves = []
        for h in range(rows // blk):
            lo = h * blk
            t = my_positions[r, lo : lo + blk]
            wanted = t[0] // blk - window_blocks + 1 + jnp.arange(window_blocks, dtype=jnp.int32)
            slots = slot_of_block[jnp.maximum(wanted, 0)]
            key_pos_sel = pos_blocks[slots].reshape(-1)
            valid = jnp.repeat(wanted >= 0, blk)
            before = t[:, None] - key_pos_sel[None, :]
            allowed_h = valid[None, :] & (before >= 0) & (before < window_len)
            state_h = tuple(
                lax.slice_in_dim(part, lo, lo + blk, axis=3) for part in running_state
            )
            state_h = attend_block(
                state_h,
                q_r[:, lo : lo + blk],
                keys_r[slots].reshape(1, window_blocks * blk, kv_local, head_size),
                values_r[slots].reshape(1, window_blocks * blk, kv_local, head_size),
                allowed_h[None],
            )
            halves.append(state_h)
        running_state = tuple(
            jnp.concatenate([half_state[i] for half_state in halves], axis=3) for i in range(3)
        )
        _, denom_final, numer_final = running_state
        attended_r = (numer_final / denom_final[..., None]).astype(jnp.bfloat16)
        attended_parts.append(
            jnp.transpose(attended_r, (0, 3, 1, 2, 4)).reshape(
                rows, kv_local * group_size * head_size
            )
        )
    attended = jnp.concatenate(attended_parts, axis=0)
    partial_out = lax.dot_general(
        attended,
        w_out_full,
        (((1,), (1,)), ((), ())),
        preferred_element_type=jnp.float32,
    )
    mixed = lax.psum_scatter(
        partial_out.reshape(requests, rows, width).astype(jnp.bfloat16),
        FSDP,
        scatter_dimension=2,
        tiled=True,
    )
    return (mixed, new_keys, new_values)


def solution(mesh):
    n_fsdp = mesh.shape["fsdp"]
    n_seq = mesh.shape["seq"]
    n_core = 2
    n_zlo = n_fsdp // n_core
    ny = 4
    nz = 2
    nx = n_seq // (ny * nz)
    fine = Mesh(mesh.devices.reshape(n_zlo, n_core, nx, nz, ny), ("z_lo", "core", "x", "z_hi", "y"))
    placed = (
        P(None, SEQ, None),
        P(),
        P(),
        P(None, SEQ, FSDP, None),
        P(None, SEQ, FSDP, None),
        P(SEQ, FSDP),
        P(SEQ, FSDP),
        P(SEQ, FSDP),
        P(SEQ, FSDP),
    )

    def body(*args):
        return shards((nx, nz, ny), *args)

    return jax.shard_map(
        body,
        mesh=fine,
        in_specs=placed,
        out_specs=(
            P(None, SEQ, FSDP),
            P(None, SEQ, FSDP, None),
            P(None, SEQ, FSDP, None),
        ),
        check_vma=False,
    )
```

```python
import math

import jax
import jax.numpy as jnp
from jax import lax
from jax.sharding import Mesh
from jax.sharding import PartitionSpec as P


SINKS = 4
NEGATIVE = -1e30

SEQ = ("x", "z_hi", "y")
FSDP = ("z_lo", "core")


def attend_block(running_state, queries, key_block, value_block, allowed):
    top_old, denom_old, numer_old = running_state
    scores = jnp.einsum("rqkgd,rpkd->rkgqp", queries, key_block, preferred_element_type=jnp.float32)
    scores = scores * (1.0 / math.sqrt(queries.shape[-1]))
    visible = allowed[:, None, None, :, :]
    scores = jnp.where(visible, scores, NEGATIVE)
    top_new = jnp.maximum(top_old, jnp.max(scores, axis=-1))
    rescale = jnp.exp(top_old - top_new)
    weights = jnp.exp(scores - top_new[..., None])
    denom_new = denom_old * rescale + jnp.sum(weights, axis=-1)
    numer_new = numer_old * rescale[..., None] + jnp.einsum(
        "rkgqp,rpkd->rkgqd",
        weights.astype(jnp.bfloat16),
        value_block,
        preferred_element_type=jnp.float32,
    )
    return (top_new, denom_new, numer_new)


def z_first_pair(piece, z_index, use_permute):
    if use_permute:
        other = lax.ppermute(piece, "z_hi", [(0, 1), (1, 0)])
        return jnp.where(z_index == 0, jnp.stack([piece, other]), jnp.stack([other, piece]))
    return lax.all_gather(piece, "z_hi", axis=0, tiled=False)


def gather_seq(piece, z_index, use_permute):
    if use_permute:
        other = lax.ppermute(piece, "z_hi", [(0, 1), (1, 0)])
        pair = jnp.where(z_index == 0, jnp.stack([piece, other]), jnp.stack([other, piece]))
    else:
        pair = lax.all_gather(piece, "z_hi", axis=0, tiled=False)
    gathered = lax.all_gather(pair, ("x", "y"), axis=0, tiled=False)
    return gathered.reshape(-1, piece.shape[-1])


def to_gather_order(array, axis, sizes):
    nx, nz, ny = sizes
    shape = array.shape
    split = shape[:axis] + (nx, nz, ny, shape[axis] // (nx * nz * ny)) + shape[axis + 1 :]
    perm = list(range(len(split)))
    perm[axis + 1], perm[axis + 2] = perm[axis + 2], perm[axis + 1]
    return jnp.transpose(array.reshape(split), perm).reshape(shape)


def from_gather_order(array, axis, sizes):
    nx, nz, ny = sizes
    shape = array.shape
    split = shape[:axis] + (nx, ny, nz, shape[axis] // (nx * nz * ny)) + shape[axis + 1 :]
    perm = list(range(len(split)))
    perm[axis + 1], perm[axis + 2] = perm[axis + 2], perm[axis + 1]
    return jnp.transpose(array.reshape(split), perm).reshape(shape)


def shards(
    sizes, tokens, positions, cached_len, cache_keys, cache_values, w_query, w_key, w_value, w_out_t
):
    requests, rows, width = tokens.shape
    head_size = cache_keys.shape[3]
    kv_local = cache_keys.shape[2]
    group_size = w_query.shape[1] // (kv_local * head_size)
    nx, nz, ny = sizes
    z_index = lax.axis_index("z_hi")
    seq_index = (lax.axis_index("x") * nz + z_index) * ny + lax.axis_index("y")
    seq_count = nx * nz * ny
    window_len = rows * seq_count // 2
    my_positions = lax.dynamic_slice_in_dim(positions, seq_index * rows, rows, 1)
    flat_tokens = to_gather_order(tokens.reshape(requests * rows, width), 1, sizes)

    q_cols = w_query.shape[1]
    k_cols = w_key.shape[1]
    o_cols = w_out_t.shape[1]
    cache_k_local = jnp.transpose(cache_keys, (1, 0, 2, 3)).reshape(rows, -1)
    cache_v_local = jnp.transpose(cache_values, (1, 0, 2, 3)).reshape(rows, -1)
    packed = jnp.concatenate([w_query, w_key, w_value, w_out_t], axis=1)
    gathered = gather_seq(packed, z_index, False)
    total_rows = gathered.shape[0]
    offs = [0]
    for c in (q_cols, k_cols, k_cols, o_cols):
        offs.append(offs[-1] + c)

    x_index = lax.axis_index("x")
    y_index = lax.axis_index("y")
    cache_pair = z_first_pair(
        jnp.concatenate([cache_k_local, cache_v_local], axis=1), z_index, True
    )
    cache_blocks = [cache_pair]
    block_sources = [(x_index, y_index)]
    for dx in range(nx):
        for dy in range(ny):
            if dx == 0 and dy == 0:
                continue
            perm = [
                (sx * ny + sy, ((sx + dx) % nx) * ny + (sy + dy) % ny)
                for sx in range(nx)
                for sy in range(ny)
            ]
            cache_blocks.append(lax.ppermute(cache_pair, ("x", "y"), perm))
            block_sources.append(((x_index - dx) % nx, (y_index - dy) % ny))
    cache_gathered = jnp.stack(cache_blocks).reshape(total_rows, -1)
    source_x = jnp.stack([sx for sx, _ in block_sources])
    source_y = jnp.stack([sy for _, sy in block_sources])
    seq_of_block = (source_x[:, None] * nz + jnp.arange(nz)[None, :]) * ny + source_y[:, None]
    cache_pos = (
        seq_of_block[:, :, None] * rows + jnp.arange(rows, dtype=jnp.int32)[None, None, :]
    ).reshape(total_rows)
    offs.append(offs[-1] + cache_k_local.shape[1])
    offs.append(offs[-1] + cache_v_local.shape[1])
    flat_tokens, cache_gathered = lax.optimization_barrier((flat_tokens, cache_gathered))
    w_qkv = gathered[:, : offs[3]]
    w_out_full = from_gather_order(gathered[:, offs[3] : offs[4]], 0, sizes)
    kv_cols = kv_local * head_size

    kv_new = jnp.dot(
        flat_tokens, w_qkv[:, q_cols:], preferred_element_type=jnp.float32
    ).astype(jnp.bfloat16)
    new_keys = kv_new[:, :k_cols].reshape(requests, rows, kv_local, head_size)
    new_values = kv_new[:, k_cols:].reshape(requests, rows, kv_local, head_size)
    queries = jnp.dot(
        flat_tokens, w_qkv[:, :q_cols], preferred_element_type=jnp.float32
    ).astype(jnp.bfloat16)
    queries = queries.reshape(requests, rows, kv_local, group_size, head_size)

    new_k_local = jnp.transpose(new_keys, (1, 0, 2, 3)).reshape(rows, -1)
    new_v_local = jnp.transpose(new_values, (1, 0, 2, 3)).reshape(rows, -1)
    new_gathered = gather_seq(jnp.concatenate([new_k_local, new_v_local], axis=1), z_index, True)
    half = new_k_local.shape[1]

    key_pos = cache_pos[None, None, :]
    new_pos = to_gather_order(positions, 1, sizes)
    lengths = cached_len[:, None]
    window_floor = lengths + my_positions - window_len
    cache_allowed = (key_pos < lengths[:, :, None]) & (
        (key_pos < SINKS) | (key_pos > window_floor[:, :, None])
    )
    before = my_positions[:, :, None] - new_pos[:, None, :]
    new_allowed = (before >= 0) & (before < window_len)

    def block_of(source, offset, r):
        piece = source[:, offset + r * kv_cols : offset + (r + 1) * kv_cols]
        return piece.reshape(1, total_rows, kv_local, head_size)

    attended_parts = []
    for r in range(requests):
        running_state = (
            jnp.full((1, kv_local, group_size, rows), NEGATIVE, jnp.float32),
            jnp.zeros((1, kv_local, group_size, rows), jnp.float32),
            jnp.zeros((1, kv_local, group_size, rows, head_size), jnp.float32),
        )
        q_r = queries[r : r + 1]
        running_state = attend_block(
            running_state,
            q_r,
            block_of(cache_gathered, 0, r),
            block_of(cache_gathered, offs[5] - offs[4], r),
            cache_allowed[r : r + 1],
        )
        running_state = attend_block(
            running_state,
            q_r,
            block_of(new_gathered, 0, r),
            block_of(new_gathered, half, r),
            new_allowed[r : r + 1],
        )
        _, denom_final, numer_final = running_state
        attended_r = (numer_final / denom_final[..., None]).astype(jnp.bfloat16)
        attended_parts.append(
            jnp.transpose(attended_r, (0, 3, 1, 2, 4)).reshape(
                rows, kv_local * group_size * head_size
            )
        )
    attended = jnp.concatenate(attended_parts, axis=0)
    partial_out = lax.dot_general(
        attended,
        w_out_full,
        (((1,), (1,)), ((), ())),
        preferred_element_type=jnp.float32,
    )
    mixed = lax.psum_scatter(
        partial_out.reshape(requests, rows, width).astype(jnp.bfloat16),
        FSDP,
        scatter_dimension=2,
        tiled=True,
    )
    return (mixed, new_keys, new_values)


def solution(mesh):
    n_fsdp = mesh.shape["fsdp"]
    n_seq = mesh.shape["seq"]
    n_core = 2
    n_zlo = n_fsdp // n_core
    ny = 4
    nz = 2
    nx = n_seq // (ny * nz)
    fine = Mesh(mesh.devices.reshape(n_zlo, n_core, nx, nz, ny), ("z_lo", "core", "x", "z_hi", "y"))
    placed = (
        P(None, SEQ, None),
        P(),
        P(),
        P(None, SEQ, FSDP, None),
        P(None, SEQ, FSDP, None),
        P(SEQ, FSDP),
        P(SEQ, FSDP),
        P(SEQ, FSDP),
        P(SEQ, FSDP),
    )

    def body(*args):
        return shards((nx, nz, ny), *args)

    return jax.shard_map(
        body,
        mesh=fine,
        in_specs=placed,
        out_specs=(
            P(None, SEQ, FSDP),
            P(None, SEQ, FSDP, None),
            P(None, SEQ, FSDP, None),
        ),
        check_vma=False,
    )
```

```python
import math

import jax
import jax.numpy as jnp
from jax import lax
from jax.sharding import Mesh
from jax.sharding import PartitionSpec as P


SINKS = 4
NEGATIVE = -1e30

SEQ = ("x", "z_hi", "y")
FSDP = ("z_lo", "core")


def attend_block(running_state, queries, key_block, value_block, allowed):
    top_old, denom_old, numer_old = running_state
    scores = jnp.einsum("rqkgd,rpkd->rkgqp", queries, key_block, preferred_element_type=jnp.float32)
    scores = scores * (1.0 / math.sqrt(queries.shape[-1]))
    visible = allowed[:, None, None, :, :]
    scores = jnp.where(visible, scores, NEGATIVE)
    top_new = jnp.maximum(top_old, jnp.max(scores, axis=-1))
    rescale = jnp.exp(top_old - top_new)
    weights = jnp.exp(scores - top_new[..., None])
    denom_new = denom_old * rescale + jnp.sum(weights, axis=-1)
    numer_new = numer_old * rescale[..., None] + jnp.einsum(
        "rkgqp,rpkd->rkgqd",
        weights.astype(jnp.bfloat16),
        value_block,
        preferred_element_type=jnp.float32,
    )
    return (top_new, denom_new, numer_new)


def gather_seq(piece, use_permute):
    if use_permute:
        other = lax.ppermute(piece, "z_hi", [(0, 1), (1, 0)])
        pair = jnp.stack([piece, other])
    else:
        pair = lax.all_gather(piece, "z_hi", axis=0, tiled=False)
    gathered = lax.all_gather(pair, ("x", "y"), axis=0, tiled=False)
    return gathered.reshape(-1, piece.shape[-1])


def to_gather_order(array, axis, sizes):
    nx, nz, ny = sizes
    shape = array.shape
    split = shape[:axis] + (nx, nz, ny, shape[axis] // (nx * nz * ny)) + shape[axis + 1 :]
    perm = list(range(len(split)))
    perm[axis + 1], perm[axis + 2] = perm[axis + 2], perm[axis + 1]
    return jnp.transpose(array.reshape(split), perm).reshape(shape)


def from_gather_order(array, axis, sizes):
    nx, nz, ny = sizes
    shape = array.shape
    split = shape[:axis] + (nx, ny, nz, shape[axis] // (nx * nz * ny)) + shape[axis + 1 :]
    perm = list(range(len(split)))
    perm[axis + 1], perm[axis + 2] = perm[axis + 2], perm[axis + 1]
    return jnp.transpose(array.reshape(split), perm).reshape(shape)


def shards(
    sizes, tokens, positions, cached_len, cache_keys, cache_values, w_query, w_key, w_value, w_out_t
):
    requests, rows, width = tokens.shape
    head_size = cache_keys.shape[3]
    kv_local = cache_keys.shape[2]
    group_size = w_query.shape[1] // (kv_local * head_size)
    nx, nz, ny = sizes
    z_index = lax.axis_index("z_hi")
    seq_index = (lax.axis_index("x") * nz + z_index) * ny + lax.axis_index("y")
    seq_count = nx * nz * ny
    window_len = rows * seq_count // 2
    my_positions = lax.dynamic_slice_in_dim(positions, seq_index * rows, rows, 1)
    flat_tokens = to_gather_order(tokens.reshape(requests * rows, width), 1, sizes)

    q_cols = w_query.shape[1]
    k_cols = w_key.shape[1]
    o_cols = w_out_t.shape[1]
    cache_k_local = jnp.transpose(cache_keys, (1, 0, 2, 3)).reshape(rows, -1)
    cache_v_local = jnp.transpose(cache_values, (1, 0, 2, 3)).reshape(rows, -1)
    packed = jnp.concatenate(
        [w_query, w_key, w_value, w_out_t, cache_k_local, cache_v_local], axis=1
    )
    gathered = gather_seq(packed, False)
    total_rows = gathered.shape[0]
    offs = [0]
    for c in (q_cols, k_cols, k_cols, o_cols, cache_k_local.shape[1], cache_v_local.shape[1]):
        offs.append(offs[-1] + c)
    w_qkv = gathered[:, : offs[3]]
    w_out_full = from_gather_order(gathered[:, offs[3] : offs[4]], 0, sizes)
    kv_cols = kv_local * head_size

    kv_new = jnp.dot(
        flat_tokens, w_qkv[:, q_cols:], preferred_element_type=jnp.float32
    ).astype(jnp.bfloat16)
    new_keys = kv_new[:, :k_cols].reshape(requests, rows, kv_local, head_size)
    new_values = kv_new[:, k_cols:].reshape(requests, rows, kv_local, head_size)
    queries = jnp.dot(
        flat_tokens, w_qkv[:, :q_cols], preferred_element_type=jnp.float32
    ).astype(jnp.bfloat16)
    queries = queries.reshape(requests, rows, kv_local, group_size, head_size)

    new_k_local = jnp.transpose(new_keys, (1, 0, 2, 3)).reshape(rows, -1)
    new_v_local = jnp.transpose(new_values, (1, 0, 2, 3)).reshape(rows, -1)
    new_gathered = gather_seq(jnp.concatenate([new_k_local, new_v_local], axis=1), True)
    half = new_k_local.shape[1]

    key_pos = to_gather_order(jnp.arange(total_rows, dtype=jnp.int32), 0, sizes)
    key_pos = key_pos[None, None, :]
    new_pos = to_gather_order(positions, 1, sizes)
    pos_pairs = new_pos.reshape(requests, nx * ny, nz, rows)
    new_pos = jnp.where(z_index == 0, pos_pairs, pos_pairs[:, :, ::-1]).reshape(new_pos.shape)
    lengths = cached_len[:, None]
    window_floor = lengths + my_positions - window_len
    cache_allowed = (key_pos < lengths[:, :, None]) & (
        (key_pos < SINKS) | (key_pos > window_floor[:, :, None])
    )
    before = my_positions[:, :, None] - new_pos[:, None, :]
    new_allowed = (before >= 0) & (before < window_len)

    def block_of(source, offset, r):
        piece = source[:, offset + r * kv_cols : offset + (r + 1) * kv_cols]
        return piece.reshape(1, total_rows, kv_local, head_size)

    attended_parts = []
    for r in range(requests):
        running_state = (
            jnp.full((1, kv_local, group_size, rows), NEGATIVE, jnp.float32),
            jnp.zeros((1, kv_local, group_size, rows), jnp.float32),
            jnp.zeros((1, kv_local, group_size, rows, head_size), jnp.float32),
        )
        q_r = queries[r : r + 1]
        running_state = attend_block(
            running_state,
            q_r,
            block_of(gathered, offs[4], r),
            block_of(gathered, offs[5], r),
            cache_allowed[r : r + 1],
        )
        running_state = attend_block(
            running_state,
            q_r,
            block_of(new_gathered, 0, r),
            block_of(new_gathered, half, r),
            new_allowed[r : r + 1],
        )
        _, denom_final, numer_final = running_state
        attended_r = (numer_final / denom_final[..., None]).astype(jnp.bfloat16)
        attended_parts.append(
            jnp.transpose(attended_r, (0, 3, 1, 2, 4)).reshape(
                rows, kv_local * group_size * head_size
            )
        )
    attended = jnp.concatenate(attended_parts, axis=0)
    partial_out = lax.dot_general(
        attended,
        w_out_full,
        (((1,), (1,)), ((), ())),
        preferred_element_type=jnp.float32,
    )
    mixed = lax.psum_scatter(
        partial_out.reshape(requests, rows, width).astype(jnp.bfloat16),
        FSDP,
        scatter_dimension=2,
        tiled=True,
    )
    return (mixed, new_keys, new_values)


def solution(mesh):
    n_fsdp = mesh.shape["fsdp"]
    n_seq = mesh.shape["seq"]
    n_core = 2
    n_zlo = n_fsdp // n_core
    ny = 4
    nz = 2
    nx = n_seq // (ny * nz)
    fine = Mesh(mesh.devices.reshape(n_zlo, n_core, nx, nz, ny), ("z_lo", "core", "x", "z_hi", "y"))
    placed = (
        P(None, SEQ, None),
        P(),
        P(),
        P(None, SEQ, FSDP, None),
        P(None, SEQ, FSDP, None),
        P(SEQ, FSDP),
        P(SEQ, FSDP),
        P(SEQ, FSDP),
        P(SEQ, FSDP),
    )

    def body(*args):
        return shards((nx, nz, ny), *args)

    return jax.shard_map(
        body,
        mesh=fine,
        in_specs=placed,
        out_specs=(
            P(None, SEQ, FSDP),
            P(None, SEQ, FSDP, None),
            P(None, SEQ, FSDP, None),
        ),
        check_vma=False,
    )
```

```python
import math

import jax
import jax.numpy as jnp
from jax import lax
from jax.sharding import Mesh
from jax.sharding import PartitionSpec as P


SINKS = 4
NEGATIVE = -1e30

SEQ = ("x", "z_hi", "y")
FSDP = ("z_lo", "core")


def attend_block(running_state, queries, key_block, value_block, allowed):
    top_old, denom_old, numer_old = running_state
    scores = jnp.einsum("rqkgd,rpkd->rkgqp", queries, key_block, preferred_element_type=jnp.float32)
    scale = 1.0 / math.sqrt(queries.shape[-1])
    visible = allowed[:, None, None, :, :]
    scores = jnp.where(visible, scores, NEGATIVE)
    top_new = jnp.maximum(top_old, jnp.max(scores, axis=-1))
    rescale = jnp.exp((top_old - top_new) * scale)
    weights = jnp.exp((scores - top_new[..., None]) * scale)
    denom_new = denom_old * rescale + jnp.sum(weights, axis=-1)
    numer_new = numer_old * rescale[..., None] + jnp.einsum(
        "rkgqp,rpkd->rkgqd",
        weights.astype(jnp.bfloat16),
        value_block,
        preferred_element_type=jnp.float32,
    )
    return (top_new, denom_new, numer_new)


def gather_seq(piece, z_index, use_permute):
    if use_permute:
        other = lax.ppermute(piece, "z_hi", [(0, 1), (1, 0)])
        pair = jnp.where(z_index == 0, jnp.stack([piece, other]), jnp.stack([other, piece]))
    else:
        pair = lax.all_gather(piece, "z_hi", axis=0, tiled=False)
    gathered = lax.all_gather(pair, ("x", "y"), axis=0, tiled=False)
    return gathered.reshape(-1, piece.shape[-1])


def to_gather_order(array, axis, sizes):
    nx, nz, ny = sizes
    shape = array.shape
    split = shape[:axis] + (nx, nz, ny, shape[axis] // (nx * nz * ny)) + shape[axis + 1 :]
    perm = list(range(len(split)))
    perm[axis + 1], perm[axis + 2] = perm[axis + 2], perm[axis + 1]
    return jnp.transpose(array.reshape(split), perm).reshape(shape)


def from_gather_order(array, axis, sizes):
    nx, nz, ny = sizes
    shape = array.shape
    split = shape[:axis] + (nx, ny, nz, shape[axis] // (nx * nz * ny)) + shape[axis + 1 :]
    perm = list(range(len(split)))
    perm[axis + 1], perm[axis + 2] = perm[axis + 2], perm[axis + 1]
    return jnp.transpose(array.reshape(split), perm).reshape(shape)


def shards(
    sizes, tokens, positions, cached_len, cache_keys, cache_values, w_query, w_key, w_value, w_out_t
):
    requests, rows, width = tokens.shape
    head_size = cache_keys.shape[3]
    kv_local = cache_keys.shape[2]
    group_size = w_query.shape[1] // (kv_local * head_size)
    nx, nz, ny = sizes
    z_index = lax.axis_index("z_hi")
    seq_index = (lax.axis_index("x") * nz + z_index) * ny + lax.axis_index("y")
    seq_count = nx * nz * ny
    window_len = rows * seq_count // 2
    my_positions = lax.dynamic_slice_in_dim(positions, seq_index * rows, rows, 1)
    flat_tokens = to_gather_order(tokens.reshape(requests * rows, width), 1, sizes)

    q_cols = w_query.shape[1]
    k_cols = w_key.shape[1]
    o_cols = w_out_t.shape[1]
    cache_k_local = jnp.transpose(cache_keys, (1, 0, 2, 3)).reshape(rows, -1)
    cache_v_local = jnp.transpose(cache_values, (1, 0, 2, 3)).reshape(rows, -1)
    packed = jnp.concatenate(
        [w_query, w_key, w_value, w_out_t, cache_k_local, cache_v_local], axis=1
    )
    gathered = gather_seq(packed, z_index, False)
    total_rows = gathered.shape[0]
    offs = [0]
    for c in (q_cols, k_cols, k_cols, o_cols, cache_k_local.shape[1], cache_v_local.shape[1]):
        offs.append(offs[-1] + c)
    w_qkv = gathered[:, : offs[3]]
    w_out_full = from_gather_order(gathered[:, offs[3] : offs[4]], 0, sizes)
    kv_cols = kv_local * head_size

    kv_new = jnp.dot(
        flat_tokens, w_qkv[:, q_cols:], preferred_element_type=jnp.float32
    ).astype(jnp.bfloat16)
    new_keys = kv_new[:, :k_cols].reshape(requests, rows, kv_local, head_size)
    new_values = kv_new[:, k_cols:].reshape(requests, rows, kv_local, head_size)
    queries = jnp.dot(
        flat_tokens, w_qkv[:, :q_cols], preferred_element_type=jnp.float32
    ).astype(jnp.bfloat16)
    queries = queries.reshape(requests, rows, kv_local, group_size, head_size)

    new_k_local = jnp.transpose(new_keys, (1, 0, 2, 3)).reshape(rows, -1)
    new_v_local = jnp.transpose(new_values, (1, 0, 2, 3)).reshape(rows, -1)
    new_gathered = gather_seq(jnp.concatenate([new_k_local, new_v_local], axis=1), z_index, True)
    half = new_k_local.shape[1]

    key_pos = to_gather_order(jnp.arange(total_rows, dtype=jnp.int32), 0, sizes)
    key_pos = key_pos[None, None, :]
    new_pos = to_gather_order(positions, 1, sizes)
    lengths = cached_len[:, None]
    window_floor = lengths + my_positions - window_len
    cache_allowed = (key_pos < lengths[:, :, None]) & (
        (key_pos < SINKS) | (key_pos > window_floor[:, :, None])
    )
    before = my_positions[:, :, None] - new_pos[:, None, :]
    new_allowed = (before >= 0) & (before < window_len)

    def block_of(source, offset, r):
        piece = source[:, offset + r * kv_cols : offset + (r + 1) * kv_cols]
        return piece.reshape(1, total_rows, kv_local, head_size)

    attended_parts = []
    for r in range(requests):
        running_state = (
            jnp.full((1, kv_local, group_size, rows), NEGATIVE, jnp.float32),
            jnp.zeros((1, kv_local, group_size, rows), jnp.float32),
            jnp.zeros((1, kv_local, group_size, rows, head_size), jnp.float32),
        )
        q_r = queries[r : r + 1]
        running_state = attend_block(
            running_state,
            q_r,
            block_of(gathered, offs[4], r),
            block_of(gathered, offs[5], r),
            cache_allowed[r : r + 1],
        )
        running_state = attend_block(
            running_state,
            q_r,
            block_of(new_gathered, 0, r),
            block_of(new_gathered, half, r),
            new_allowed[r : r + 1],
        )
        _, denom_final, numer_final = running_state
        attended_r = (numer_final / denom_final[..., None]).astype(jnp.bfloat16)
        attended_parts.append(
            jnp.transpose(attended_r, (0, 3, 1, 2, 4)).reshape(
                rows, kv_local * group_size * head_size
            )
        )
    attended = jnp.concatenate(attended_parts, axis=0)
    partial_out = lax.dot_general(
        attended,
        w_out_full,
        (((1,), (1,)), ((), ())),
        preferred_element_type=jnp.float32,
    )
    mixed = lax.psum_scatter(
        partial_out.reshape(requests, rows, width).astype(jnp.bfloat16),
        FSDP,
        scatter_dimension=2,
        tiled=True,
    )
    return (mixed, new_keys, new_values)


def solution(mesh):
    n_fsdp = mesh.shape["fsdp"]
    n_seq = mesh.shape["seq"]
    n_core = 2
    n_zlo = n_fsdp // n_core
    ny = 4
    nz = 2
    nx = n_seq // (ny * nz)
    fine = Mesh(mesh.devices.reshape(n_zlo, n_core, nx, nz, ny), ("z_lo", "core", "x", "z_hi", "y"))
    placed = (
        P(None, SEQ, None),
        P(),
        P(),
        P(None, SEQ, FSDP, None),
        P(None, SEQ, FSDP, None),
        P(SEQ, FSDP),
        P(SEQ, FSDP),
        P(SEQ, FSDP),
        P(SEQ, FSDP),
    )

    def body(*args):
        return shards((nx, nz, ny), *args)

    return jax.shard_map(
        body,
        mesh=fine,
        in_specs=placed,
        out_specs=(
            P(None, SEQ, FSDP),
            P(None, SEQ, FSDP, None),
            P(None, SEQ, FSDP, None),
        ),
        check_vma=False,
    )
```
